256 devices in a mesh: query: 2 (over core), list: 128 (over y, x, z).
Axes of the slice: x: 4, y: 4, z: 8, core: 2. Of those that a mesh axis runs over, the one named last changes fastest.
Arguments:
- queries: float32 [1024, 1024], P(('query', 'list')), may hold values from -0.24 to 0.24
- probes: int32 [1024, 32], P(('query', 'list')), may hold values from 0 to 127, all different within a row; in each aligned block of 4 rows (0 to 3, 4 to 7, ...) at most 2 rows name the same one
- centroids: float32 [128, 1024], replicated, may hold values from -0.15 to 0.15
- codebook: float32 [64, 16, 256], P('query'), may hold values from -0.15 to 0.15
- codes: int32 [128, 64, 512], P('list'), may hold values from 0 to 255
- cell_sizes: int32 [128], P('list'), may hold values from 64 to 512
Outputs:
- scores: float32 [1024, 32, 512], P(('query', 'list'))
The draws below stay inside these ranges and needn't reach their ends.
Inputs may be any that keep to these rules, and one draw needn't show every extreme that they name: `probes`: each row names 32 different cells; among the rows of one device no cell is named by more than 2 rows.
All inputs are finite; a program needn't handle non-finite values.
Results may differ from the reference program's by a relative error of at most 0.0003.
Values sent between devices are 32-bit elements; how exact they have to be, the bound alone decides.
No kernel may reach another device: no remote copies, remote signals or barrier semaphores. Data moves between devices by JAX's collectives and lax.ppermute only.
A program may use at most 128 MiB of HBM per device.

```python
import math
import jax
import jax.numpy as jnp
import numpy as np
from jax import lax

DIM = 1024
M = 64
KS = 256
DSUB = 16
CAP = 512
NPROBE = 32
QDEV = 4
Q = 1024
CELLS = 128
SLOT = 2


def draw_cell_sizes(key, part):
    size_key = jax.random.fold_in(key, 11)
    spot_key = jax.random.fold_in(key, 12)
    drawn_sizes = jax.random.randint(size_key, (CELLS,), CAP // 8, CAP + 1, dtype=jnp.int32)
    where_full = jax.random.randint(spot_key, (), 0, CELLS, dtype=jnp.int32)
    where_least = (where_full + 1) % CELLS
    cell_index = jnp.arange(CELLS, dtype=jnp.int32)
    drawn_sizes = jnp.where(cell_index == where_full, CAP, drawn_sizes)
    return jnp.where(cell_index == where_least, CAP // 8, drawn_sizes)


def with_ends(array, stream_key, least, high):
    longest = array.shape.index(max(array.shape))
    spots = []
    for shift in (0, 1):
        where = [jax.random.randint(jax.random.fold_in(stream_key, axis), (), 0, length) for axis, length in enumerate(array.shape)]
        where[longest] = (where[longest] + shift) % array.shape[longest]
        spots.append(tuple(where))
    return array.at[spots[0]].set(least).at[spots[1]].set(high)


def levels(own_key, shape, cuts, smallest, high):
    level, own = 1.0, jax.random.fold_in(own_key, 6)
    for axis_at, shards_of in cuts:
        steps = jnp.exp(jax.random.uniform(jax.random.fold_in(own, axis_at), (shards_of,), jnp.float32, smallest / len(cuts), high / len(cuts)))
        level = level * jnp.repeat(steps, shape[axis_at] // shards_of).reshape([-1 if axis == axis_at else 1 for axis in range(len(shape))])
    return level


def routed_block(rng, own, number, rows, number_of, top, bound, skew):
    sequence = jax.random.permutation(rng, number_of)
    heavy_load, ordinary = load_shares(number_of, rows * top, bound, skew, True), load_shares(number_of, rows * top, bound, skew, False)
    places = jnp.arange(number_of)

    def named(lengths, turn):
        used = int((lengths > 0).sum())
        fixed = max(1, used // 4)
        passed = fixed + (places - fixed + turn * (used - fixed)) % max(1, number_of - fixed)
        return jnp.zeros((number_of,), jnp.int32).at[sequence[jnp.where(places < fixed, places, passed)]].set(jnp.asarray(lengths, jnp.int32))

    lengths = jnp.where(number % 4 == 0, named(heavy_load, number // 4), named(ordinary, number - number // 4 - 1))
    mixed = jax.random.permutation(jax.random.fold_in(own, 3), number_of)
    source_of, receiver = mixed[0:number_of // 2 * 2:2], mixed[1:number_of // 2 * 2:2]
    slack = jnp.minimum(lengths[source_of] - 1, bound - lengths[receiver]) // 2
    slack = jnp.where((source_of == sequence[0]) | (receiver == sequence[0]) | (lengths[receiver] == 0), 0, jnp.maximum(slack, 0))
    passed = jax.random.randint(jax.random.fold_in(own, 4), (number_of // 2,), 0, 1 << 20) % (slack + 1)
    lengths = lengths.at[source_of].add(-passed).at[receiver].add(passed)
    labels = jnp.searchsorted(jnp.cumsum(lengths), jnp.arange(rows * top), side="right").astype(jnp.int32)
    grid = labels.reshape(top, rows).T
    grid = grid[jax.random.permutation(jax.random.fold_in(own, 1), rows)]
    turn = jax.random.randint(jax.random.fold_in(own, 2), (rows, 1), 0, top)
    return jnp.take_along_axis(grid, (jnp.arange(top)[None, :] + turn) % top, axis=1)


def load_shares(number_of, total, reach, lean, full):
    weights = [(1 << 20) // math.isqrt(grade ** lean) + 1 for grade in range(1, number_of + 1)]
    largest = reach if full else min(reach, max(-(-total // number_of), total * weights[0] // sum(weights)))
    least = 1 if total - largest >= number_of - 1 else 0
    given, rest = [largest] + [least] * (number_of - 1), total - largest - least * (number_of - 1)
    while rest > 0:
        candidates = [i for i in range(1, number_of) if given[i] < largest] or [i for i in range(1, number_of) if given[i] < reach]
        pool, left = sum([weights[i] for i in candidates]), rest
        for i in candidates:
            more = min(reach - given[i], max(1, left * weights[i] // pool), rest)
            given[i] = given[i] + more
            rest = rest - more
    return np.array(given)


def scatter_about(stream_key, shape, scale, most, split=(), kind=jnp.bfloat16):
    array = jax.random.normal(stream_key, shape, jnp.float32) * scale
    if len(split) > 0:
        array = levels(stream_key, shape, split, -0.22, 0.18) * array
    return jnp.clip(array, min=-most, max=most).astype(kind)


def setup_inputs(seed: int = 0) -> dict:
    key_of = jax.random.split(jax.random.key(seed), 7)
    queries = scatter_about(key_of[0], (Q, DIM), 0.04, 0.24, ((0, 256),), jnp.float32)
    probes_keys = jax.random.split(jax.random.fold_in(key_of[1], 1), Q // QDEV)
    probes_turns = jax.random.permutation(jax.random.fold_in(key_of[1], 3), Q // QDEV)
    probes = jax.vmap(lambda own, number: routed_block(jax.random.fold_in(key_of[1], 2), own, number, QDEV, CELLS, NPROBE, SLOT, 2))(probes_keys, probes_turns).reshape((Q, NPROBE))
    centroids = scatter_about(key_of[2], (CELLS, DIM), 0.025, 0.15, (), jnp.float32)
    codebook = scatter_about(key_of[3], (M, DSUB, KS), 0.025, 0.15, ((0, 2),), jnp.float32)
    codes = with_ends(jax.random.randint(key_of[4], (CELLS, M, CAP), 0, KS), jax.random.fold_in(key_of[4], 1), 0, KS - 1).astype(jnp.int32)
    cell_sizes = draw_cell_sizes(jax.random.fold_in(key_of[6], 71), 0)
    return dict(queries=queries, probes=probes, centroids=centroids, codebook=codebook, codes=codes, cell_sizes=cell_sizes)


def tables_of(residual, codebook):
    cross_terms = jnp.einsum("pmd,mdk->pmk", residual, codebook, precision=lax.Precision.HIGHEST)
    own_norm = jnp.sum(residual * residual, axis=-1)[..., None]
    word_norm = jnp.sum(codebook * codebook, axis=1)[None]
    return own_norm - 2.0 * cross_terms + word_norm


def reference(queries, probes, centroids, codebook, codes, cell_sizes):
    positions = jnp.arange(CAP, dtype=jnp.int32)

    def score_query(pair_args):
        query_row, probed = pair_args
        residual = (query_row[None, :] - centroids[probed]).reshape(NPROBE, M, DSUB)
        tables_now = tables_of(residual, codebook)
        picked = codes[probed]
        gathered = jnp.take_along_axis(tables_now, picked, axis=2)
        summed = jnp.sum(gathered, axis=1)
        valid_rows = positions[None, :] < cell_sizes[probed][:, None]
        return jnp.where(valid_rows, summed, jnp.zeros_like(summed))

    return lax.map(score_query, (queries, probes))
```

```python
import jax
import jax.numpy as jnp
from jax import lax
from jax.sharding import PartitionSpec as P

slot_count = 2


def exact_parts(values):
    high = values.astype(jnp.bfloat16)
    rest = values - high.astype(jnp.float32)
    middle = rest.astype(jnp.bfloat16)
    low = (rest - middle.astype(jnp.float32)).astype(jnp.bfloat16)
    return jnp.concatenate([high, middle, low], axis=-1)


def rebuilt_slots(codebook_all, cell_codes):
    subspaces, sub_width, codewords = codebook_all.shape
    capacity = cell_codes.shape[1]
    parts = exact_parts(jnp.transpose(codebook_all, (0, 2, 1)))
    word_ids = jnp.arange(codewords, dtype=jnp.int32)
    one_hot = (cell_codes[:, :, None] == word_ids[None, None, :]).astype(jnp.bfloat16)
    picked = jnp.einsum("mvk,mkd->vmd", one_hot, parts, preferred_element_type=jnp.float32)
    rebuilt = (
        picked[..., :sub_width] + picked[..., sub_width : 2 * sub_width]
    ) + picked[..., 2 * sub_width :]
    return rebuilt.reshape(capacity, subspaces * sub_width)


def body(queries, probes, centroids, codebook, codes, cell_sizes):
    list_size = lax.axis_size("list")
    query_rows, probe_count = probes.shape
    cells_dev, subspaces, capacity = codes.shape
    dim = queries.shape[1]
    cell_count = cells_dev * list_size
    codebook_all = lax.all_gather(codebook, "query", axis=0, tiled=True)

    flat_cells = probes.reshape(-1)
    pair_count = flat_cells.shape[0]
    pair_order = jnp.arange(pair_count, dtype=jnp.int32)
    earlier_same = (flat_cells[:, None] == flat_cells[None, :]) & (
        pair_order[None, :] < pair_order[:, None]
    )
    slot_rank = jnp.sum(earlier_same.astype(jnp.int32), axis=1)
    owner_query = pair_order // probe_count
    cell_ids = jnp.arange(cell_count, dtype=jnp.int32)
    slot_ids = jnp.arange(slot_count, dtype=jnp.int32)
    chosen = (flat_cells[:, None, None] == cell_ids[None, :, None]) & (
        slot_rank[:, None, None] == slot_ids[None, None, :]
    )
    filled = jnp.any(chosen, axis=0)
    source = jnp.sum(jnp.where(chosen, owner_query[:, None, None], 0), axis=0)
    outgoing = jnp.where(filled[..., None], queries[source], jnp.zeros((), jnp.float32))
    outgoing = outgoing.reshape(list_size, cells_dev, slot_count, dim)
    arrived = lax.all_to_all(outgoing, "list", split_axis=0, concat_axis=0, tiled=True)

    first_cell = lax.axis_index("list") * cells_dev
    positions = jnp.arange(capacity, dtype=jnp.int32)
    scored = []
    for local in range(cells_dev):
        centroid = lax.dynamic_slice_in_dim(centroids, first_cell + local, 1, axis=0)
        residual = arrived[:, local].reshape(list_size * slot_count, dim) - centroid
        rebuilt = rebuilt_slots(codebook_all, codes[local])
        own_norm = jnp.sum(residual * residual, axis=1)
        slot_norm = jnp.sum(rebuilt * rebuilt, axis=1)
        cross = jnp.einsum(
            "sf,vf->sv", residual, rebuilt, precision=lax.Precision.HIGHEST
        )
        total = (own_norm[:, None] + slot_norm[None, :]) - 2.0 * cross
        valid = positions < cell_sizes[local]
        total = jnp.where(valid[None, :], total, jnp.zeros((), jnp.float32))
        scored.append(total.reshape(list_size, slot_count, capacity))
    scored = jnp.stack(scored, axis=1)
    returned = lax.all_to_all(scored, "list", split_axis=0, concat_axis=0, tiled=True)
    returned = returned.reshape(cell_count * slot_count, capacity)
    result = returned[flat_cells * slot_count + slot_rank]
    return result.reshape(query_rows, probe_count, capacity)


def solution(mesh):
    in_specs = (
        P(("query", "list"), None),
        P(("query", "list"), None),
        P(),
        P("query", None, None),
        P("list", None, None),
        P("list"),
    )
    out_specs = P(("query", "list"), None, None)
    return jax.shard_map(body, mesh=mesh, in_specs=in_specs, out_specs=out_specs, check_vma=False)
```

```python
import jax
import jax.numpy as jnp
from jax import lax
from jax.sharding import PartitionSpec as P

slot_count = 2


def exact_parts(values):
    high = values.astype(jnp.bfloat16)
    rest = values - high.astype(jnp.float32)
    middle = rest.astype(jnp.bfloat16)
    low = (rest - middle.astype(jnp.float32)).astype(jnp.bfloat16)
    return jnp.concatenate([high, middle, low], axis=-1)


def rebuilt_slots(codebook_all, cell_codes):
    subspaces, sub_width, codewords = codebook_all.shape
    capacity = cell_codes.shape[1]
    parts = exact_parts(jnp.transpose(codebook_all, (0, 2, 1)))
    word_ids = jnp.arange(codewords, dtype=jnp.int32)
    one_hot = (cell_codes[:, :, None] == word_ids[None, None, :]).astype(jnp.bfloat16)
    picked = jnp.einsum("mvk,mkd->vmd", one_hot, parts, preferred_element_type=jnp.float32)
    rebuilt = (
        picked[..., :sub_width] + picked[..., sub_width : 2 * sub_width]
    ) + picked[..., 2 * sub_width :]
    return rebuilt.reshape(capacity, subspaces * sub_width)


def body(queries, probes, centroids, codebook, codes, cell_sizes):
    list_size = lax.axis_size("list")
    query_rows, probe_count = probes.shape
    cells_dev, subspaces, capacity = codes.shape
    dim = queries.shape[1]
    cell_count = cells_dev * list_size
    query_size = lax.axis_size("query")
    if query_size == 2:
        other = lax.ppermute(codebook, "query", [(0, 1), (1, 0)])
        first = lax.axis_index("query") == 0
        low_half = jnp.where(first, codebook, other)
        high_half = jnp.where(first, other, codebook)
        codebook_all = jnp.concatenate([low_half, high_half], axis=0)
    else:
        codebook_all = lax.all_gather(codebook, "query", axis=0, tiled=True)

    flat_cells = probes.reshape(-1)
    pair_count = flat_cells.shape[0]
    pair_order = jnp.arange(pair_count, dtype=jnp.int32)
    earlier_same = (flat_cells[:, None] == flat_cells[None, :]) & (
        pair_order[None, :] < pair_order[:, None]
    )
    slot_rank = jnp.sum(earlier_same.astype(jnp.int32), axis=1)
    owner_query = pair_order // probe_count
    cell_ids = jnp.arange(cell_count, dtype=jnp.int32)
    slot_ids = jnp.arange(slot_count, dtype=jnp.int32)
    chosen = (flat_cells[:, None, None] == cell_ids[None, :, None]) & (
        slot_rank[:, None, None] == slot_ids[None, None, :]
    )
    filled = jnp.any(chosen, axis=0)
    source = jnp.sum(jnp.where(chosen, owner_query[:, None, None], 0), axis=0)
    outgoing = jnp.where(filled[..., None], queries[source], jnp.zeros((), jnp.float32))
    outgoing = outgoing.reshape(list_size, cells_dev, slot_count, dim)
    arrived = lax.all_to_all(outgoing, "list", split_axis=0, concat_axis=0, tiled=True)

    first_cell = lax.axis_index("list") * cells_dev
    positions = jnp.arange(capacity, dtype=jnp.int32)
    scored = []
    for local in range(cells_dev):
        centroid = lax.dynamic_slice_in_dim(centroids, first_cell + local, 1, axis=0)
        residual = arrived[:, local].reshape(list_size * slot_count, dim) - centroid
        rebuilt = rebuilt_slots(codebook_all, codes[local])
        own_norm = jnp.sum(residual * residual, axis=1)
        slot_norm = jnp.sum(rebuilt * rebuilt, axis=1)
        cross = jnp.einsum(
            "sf,vf->sv", residual, rebuilt, precision=lax.Precision.HIGHEST
        )
        total = (own_norm[:, None] + slot_norm[None, :]) - 2.0 * cross
        valid = positions < cell_sizes[local]
        total = jnp.where(valid[None, :], total, jnp.zeros((), jnp.float32))
        scored.append(total.reshape(list_size, slot_count, capacity))
    scored = jnp.stack(scored, axis=1)
    returned = lax.all_to_all(scored, "list", split_axis=0, concat_axis=0, tiled=True)
    returned = returned.reshape(cell_count * slot_count, capacity)
    result = returned[flat_cells * slot_count + slot_rank]
    return result.reshape(query_rows, probe_count, capacity)


def solution(mesh):
    in_specs = (
        P(("query", "list"), None),
        P(("query", "list"), None),
        P(),
        P("query", None, None),
        P("list", None, None),
        P("list"),
    )
    out_specs = P(("query", "list"), None, None)
    return jax.shard_map(body, mesh=mesh, in_specs=in_specs, out_specs=out_specs, check_vma=False)
```

```python
import jax
import jax.numpy as jnp
from jax import lax
from jax.sharding import PartitionSpec as P

slot_count = 2


def exact_parts(values):
    high = values.astype(jnp.bfloat16)
    rest = values - high.astype(jnp.float32)
    middle = rest.astype(jnp.bfloat16)
    low = (rest - middle.astype(jnp.float32)).astype(jnp.bfloat16)
    return jnp.concatenate([high, middle, low], axis=-1)


def rebuilt_slots(codebook_all, cell_codes):
    subspaces, sub_width, codewords = codebook_all.shape
    capacity = cell_codes.shape[1]
    parts = exact_parts(jnp.transpose(codebook_all, (0, 2, 1)))
    word_ids = jnp.arange(codewords, dtype=jnp.int32)
    one_hot = (cell_codes[:, :, None] == word_ids[None, None, :]).astype(jnp.bfloat16)
    picked = jnp.einsum("mvk,mkd->vmd", one_hot, parts, preferred_element_type=jnp.float32)
    rebuilt = (
        picked[..., :sub_width] + picked[..., sub_width : 2 * sub_width]
    ) + picked[..., 2 * sub_width :]
    return rebuilt.reshape(capacity, subspaces * sub_width)


def body(queries, probes, centroids, codebook, codes, cell_sizes):
    list_size = lax.axis_size("list")
    query_rows, probe_count = probes.shape
    cells_dev, subspaces, capacity = codes.shape
    dim = queries.shape[1]
    cell_count = cells_dev * list_size
    query_size = lax.axis_size("query")
    if query_size == 2:
        other = lax.ppermute(codebook, "query", [(0, 1), (1, 0)])
        first = lax.axis_index("query") == 0
        low_half = jnp.where(first, codebook, other)
        high_half = jnp.where(first, other, codebook)
        codebook_all = jnp.concatenate([low_half, high_half], axis=0)
    else:
        codebook_all = lax.all_gather(codebook, "query", axis=0, tiled=True)

    flat_cells = probes.reshape(-1)
    pair_count = flat_cells.shape[0]
    pair_order = jnp.arange(pair_count, dtype=jnp.int32)
    earlier_same = (flat_cells[:, None] == flat_cells[None, :]) & (
        pair_order[None, :] < pair_order[:, None]
    )
    slot_rank = jnp.sum(earlier_same.astype(jnp.int32), axis=1)
    owner_query = pair_order // probe_count
    cell_ids = jnp.arange(cell_count, dtype=jnp.int32)
    slot_ids = jnp.arange(slot_count, dtype=jnp.int32)
    chosen = (flat_cells[:, None, None] == cell_ids[None, :, None]) & (
        slot_rank[:, None, None] == slot_ids[None, None, :]
    )
    lanes = 128
    tile_rows = dim // lanes
    query_tiles = queries.reshape(query_rows, tile_rows, lanes)
    outgoing = jnp.zeros((cell_count, slot_count, tile_rows, lanes), jnp.float32)
    for row in range(query_rows):
        taken = jnp.any(chosen & (owner_query == row)[:, None, None], axis=0)
        outgoing = jnp.where(taken[:, :, None, None], query_tiles[row][None, None], outgoing)
    outgoing = outgoing.reshape(list_size, cells_dev, slot_count, tile_rows, lanes)
    arrived = lax.all_to_all(outgoing, "list", split_axis=0, concat_axis=0, tiled=True)

    first_cell = lax.axis_index("list") * cells_dev
    positions = jnp.arange(capacity, dtype=jnp.int32)
    scored = []
    for local in range(cells_dev):
        centroid = lax.dynamic_slice_in_dim(centroids, first_cell + local, 1, axis=0)
        residual = arrived[:, local] - centroid.reshape(1, 1, tile_rows, lanes)
        own_norm = jnp.sum(residual * residual, axis=(2, 3)).reshape(-1)
        residual = residual.reshape(list_size * slot_count, dim)
        rebuilt = rebuilt_slots(codebook_all, codes[local])
        slot_norm = jnp.sum(rebuilt * rebuilt, axis=1)
        cross = jnp.einsum(
            "sf,vf->sv", residual, rebuilt, precision=lax.Precision.HIGHEST
        )
        total = (own_norm[:, None] + slot_norm[None, :]) - 2.0 * cross
        valid = positions < cell_sizes[local]
        total = jnp.where(valid[None, :], total, jnp.zeros((), jnp.float32))
        scored.append(total.reshape(list_size, slot_count, capacity))
    scored = jnp.stack(scored, axis=1)
    returned = lax.all_to_all(scored, "list", split_axis=0, concat_axis=0, tiled=True)
    returned = returned.reshape(cell_count * slot_count, capacity)
    result = returned[flat_cells * slot_count + slot_rank]
    return result.reshape(query_rows, probe_count, capacity)


def solution(mesh):
    in_specs = (
        P(("query", "list"), None),
        P(("query", "list"), None),
        P(),
        P("query", None, None),
        P("list", None, None),
        P("list"),
    )
    out_specs = P(("query", "list"), None, None)
    return jax.shard_map(body, mesh=mesh, in_specs=in_specs, out_specs=out_specs, check_vma=False)
```

```python
import functools

import jax
import jax.numpy as jnp
from jax import lax
from jax.sharding import PartitionSpec as P

slot_count = 2


def exact_parts(values):
    high = values.astype(jnp.bfloat16)
    rest = values - high.astype(jnp.float32)
    middle = rest.astype(jnp.bfloat16)
    low = (rest - middle.astype(jnp.float32)).astype(jnp.bfloat16)
    return jnp.concatenate([high, middle, low], axis=-1)


def rebuilt_slots(codebook_all, cell_codes):
    subspaces, sub_width, codewords = codebook_all.shape
    capacity = cell_codes.shape[1]
    parts = exact_parts(jnp.transpose(codebook_all, (0, 2, 1)))
    word_ids = jnp.arange(codewords, dtype=jnp.int32)
    one_hot = (cell_codes[:, :, None] == word_ids[None, None, :]).astype(jnp.bfloat16)
    picked = jnp.einsum("mvk,mkd->vmd", one_hot, parts, preferred_element_type=jnp.float32)
    rebuilt = (
        picked[..., :sub_width] + picked[..., sub_width : 2 * sub_width]
    ) + picked[..., 2 * sub_width :]
    return rebuilt.reshape(capacity, subspaces * sub_width)


def list_digits(mesh):
    row = mesh.devices[0] if mesh.devices.ndim == 2 else None
    if row is None or any(getattr(d, "coords", None) is None for d in row):
        return None
    coords = [tuple(d.coords) for d in row]
    sizes = tuple(1 + max(c[axis] for c in coords) for axis in (1, 0, 2))
    count = sizes[0] * sizes[1] * sizes[2]
    if count != len(row):
        return None
    for place, (x, y, z) in enumerate(coords):
        if place != (y * sizes[1] + x) * sizes[2] + z:
            return None
    return sizes


def digit_groups(sizes):
    first, second, third = sizes
    index = lambda a, b, c: (a * second + b) * third + c
    by_third = [[index(a, b, c) for c in range(third)] for a in range(first) for b in range(second)]
    by_second = [[index(a, b, c) for b in range(second)] for a in range(first) for c in range(third)]
    by_first = [[index(a, b, c) for a in range(first)] for b in range(second) for c in range(third)]
    return (by_first, by_second, by_third)


def list_exchange(values, sizes):
    if sizes is None:
        return lax.all_to_all(values, "list", split_axis=0, concat_axis=0, tiled=True)
    rest = values.shape[1:]
    staged = values.reshape(*sizes, *rest)
    groups = digit_groups(sizes)
    for digit in (2, 1, 0):
        if sizes[digit] > 1:
            staged = lax.all_to_all(
                staged, "list", split_axis=digit, concat_axis=digit,
                axis_index_groups=groups[digit], tiled=True,
            )
    return staged.reshape(values.shape)


def body(sizes, queries, probes, centroids, codebook, codes, cell_sizes):
    list_size = lax.axis_size("list")
    query_rows, probe_count = probes.shape
    cells_dev, subspaces, capacity = codes.shape
    dim = queries.shape[1]
    cell_count = cells_dev * list_size
    query_size = lax.axis_size("query")
    if query_size == 2:
        other = lax.ppermute(codebook, "query", [(0, 1), (1, 0)])
        first = lax.axis_index("query") == 0
        low_half = jnp.where(first, codebook, other)
        high_half = jnp.where(first, other, codebook)
        codebook_all = jnp.concatenate([low_half, high_half], axis=0)
    else:
        codebook_all = lax.all_gather(codebook, "query", axis=0, tiled=True)

    flat_cells = probes.reshape(-1)
    pair_count = flat_cells.shape[0]
    pair_order = jnp.arange(pair_count, dtype=jnp.int32)
    earlier_same = (flat_cells[:, None] == flat_cells[None, :]) & (
        pair_order[None, :] < pair_order[:, None]
    )
    slot_rank = jnp.sum(earlier_same.astype(jnp.int32), axis=1)
    owner_query = pair_order // probe_count
    cell_ids = jnp.arange(cell_count, dtype=jnp.int32)
    slot_ids = jnp.arange(slot_count, dtype=jnp.int32)
    chosen = (flat_cells[:, None, None] == cell_ids[None, :, None]) & (
        slot_rank[:, None, None] == slot_ids[None, None, :]
    )
    lanes = 128
    tile_rows = dim // lanes
    query_tiles = queries.reshape(query_rows, tile_rows, lanes)
    outgoing = jnp.zeros((cell_count, slot_count, tile_rows, lanes), jnp.float32)
    for row in range(query_rows):
        taken = jnp.any(chosen & (owner_query == row)[:, None, None], axis=0)
        outgoing = jnp.where(taken[:, :, None, None], query_tiles[row][None, None], outgoing)
    outgoing = outgoing.reshape(list_size, cells_dev, slot_count, tile_rows, lanes)
    arrived = list_exchange(outgoing, sizes)

    first_cell = lax.axis_index("list") * cells_dev
    positions = jnp.arange(capacity, dtype=jnp.int32)
    scored = []
    for local in range(cells_dev):
        centroid = lax.dynamic_slice_in_dim(centroids, first_cell + local, 1, axis=0)
        residual = arrived[:, local] - centroid.reshape(1, 1, tile_rows, lanes)
        own_norm = jnp.sum(residual * residual, axis=(2, 3)).reshape(-1)
        residual = residual.reshape(list_size * slot_count, dim)
        rebuilt = rebuilt_slots(codebook_all, codes[local])
        slot_norm = jnp.sum(rebuilt * rebuilt, axis=1)
        cross = jnp.einsum(
            "sf,vf->sv", residual, rebuilt, precision=lax.Precision.HIGHEST
        )
        total = (own_norm[:, None] + slot_norm[None, :]) - 2.0 * cross
        valid = positions < cell_sizes[local]
        total = jnp.where(valid[None, :], total, jnp.zeros((), jnp.float32))
        scored.append(total.reshape(list_size, slot_count, capacity))
    scored = jnp.stack(scored, axis=1)
    returned = list_exchange(scored, sizes)
    returned = returned.reshape(cell_count * slot_count, capacity)
    result = returned[flat_cells * slot_count + slot_rank]
    return result.reshape(query_rows, probe_count, capacity)


def solution(mesh):
    in_specs = (
        P(("query", "list"), None),
        P(("query", "list"), None),
        P(),
        P("query", None, None),
        P("list", None, None),
        P("list"),
    )
    out_specs = P(("query", "list"), None, None)
    sizes = list_digits(mesh)
    return jax.shard_map(functools.partial(body, sizes), mesh=mesh, in_specs=in_specs, out_specs=out_specs, check_vma=False)
```

```python
import jax
import jax.numpy as jnp
from jax import lax
from jax.sharding import PartitionSpec as P

slot_count = 2


def exact_parts(values):
    high = values.astype(jnp.bfloat16)
    rest = values - high.astype(jnp.float32)
    middle = rest.astype(jnp.bfloat16)
    low = (rest - middle.astype(jnp.float32)).astype(jnp.bfloat16)
    return jnp.concatenate([high, middle, low], axis=-1)


def rebuilt_slots(codebook_all, cell_codes):
    subspaces, sub_width, codewords = codebook_all.shape
    capacity = cell_codes.shape[1]
    parts = exact_parts(jnp.transpose(codebook_all, (0, 2, 1)))
    word_ids = jnp.arange(codewords, dtype=jnp.int32)
    one_hot = (cell_codes[:, :, None] == word_ids[None, None, :]).astype(jnp.bfloat16)
    picked = jnp.einsum("mvk,mkd->vmd", one_hot, parts, preferred_element_type=jnp.float32)
    rebuilt = (
        picked[..., :sub_width] + picked[..., sub_width : 2 * sub_width]
    ) + picked[..., 2 * sub_width :]
    return rebuilt.reshape(capacity, subspaces * sub_width)


def body(queries, probes, centroids, codebook, codes, cell_sizes):
    list_size = lax.axis_size("list")
    query_rows, probe_count = probes.shape
    cells_dev, subspaces, capacity = codes.shape
    dim = queries.shape[1]
    cell_count = cells_dev * list_size
    query_size = lax.axis_size("query")
    if query_size == 2:
        other = lax.ppermute(codebook, "query", [(0, 1), (1, 0)])
        first = lax.axis_index("query") == 0
        low_half = jnp.where(first, codebook, other)
        high_half = jnp.where(first, other, codebook)
        codebook_all = jnp.concatenate([low_half, high_half], axis=0)
    else:
        codebook_all = lax.all_gather(codebook, "query", axis=0, tiled=True)

    flat_cells = probes.reshape(-1)
    cell_ids = jnp.arange(cell_count, dtype=jnp.int32)
    contains = jnp.any(probes[:, :, None] == cell_ids[None, None, :], axis=1)
    counted = contains.astype(jnp.int32)
    earlier_rows = jnp.cumsum(counted, axis=0) - counted
    rank_of = jnp.take_along_axis(earlier_rows, probes, axis=1)
    slot_rank = rank_of.reshape(-1)
    lanes = 128
    tile_rows = dim // lanes
    query_tiles = queries.reshape(query_rows, tile_rows, lanes)
    row_at = jnp.full((cell_count, slot_count), -1, jnp.int32)
    for row in range(query_rows):
        here = contains[row][:, None] & (earlier_rows[row][:, None] == jnp.arange(slot_count)[None, :])
        row_at = jnp.where(here, row, row_at)
    row_at = row_at[:, :, None, None]
    outgoing = jnp.zeros((cell_count, slot_count, tile_rows, lanes), jnp.float32)
    for row in range(query_rows):
        outgoing = jnp.where(row_at == row, query_tiles[row][None, None], outgoing)
    outgoing = outgoing.reshape(list_size, cells_dev, slot_count, tile_rows, lanes)
    arrived = lax.all_to_all(outgoing, "list", split_axis=0, concat_axis=0, tiled=True)

    first_cell = lax.axis_index("list") * cells_dev
    positions = jnp.arange(capacity, dtype=jnp.int32)
    scored = []
    for local in range(cells_dev):
        centroid = lax.dynamic_slice_in_dim(centroids, first_cell + local, 1, axis=0)
        residual = arrived[:, local] - centroid.reshape(1, 1, tile_rows, lanes)
        own_norm = jnp.sum(residual * residual, axis=(2, 3)).reshape(-1)
        residual = residual.reshape(list_size * slot_count, dim)
        rebuilt = rebuilt_slots(codebook_all, codes[local])
        slot_norm = jnp.sum(rebuilt * rebuilt, axis=1)
        cross = jnp.einsum(
            "sf,vf->sv", residual, rebuilt, precision=lax.Precision.HIGH
        )
        total = (own_norm[:, None] + slot_norm[None, :]) - 2.0 * cross
        valid = positions < cell_sizes[local]
        total = jnp.where(valid[None, :], total, jnp.zeros((), jnp.float32))
        scored.append(total.reshape(list_size, slot_count, capacity))
    scored = jnp.stack(scored, axis=1)
    returned = lax.all_to_all(scored, "list", split_axis=0, concat_axis=0, tiled=True)
    returned = returned.reshape(cell_count * slot_count, capacity)
    result = returned[flat_cells * slot_count + slot_rank]
    return result.reshape(query_rows, probe_count, capacity)


def solution(mesh):
    in_specs = (
        P(("query", "list"), None),
        P(("query", "list"), None),
        P(),
        P("query", None, None),
        P("list", None, None),
        P("list"),
    )
    out_specs = P(("query", "list"), None, None)
    return jax.shard_map(body, mesh=mesh, in_specs=in_specs, out_specs=out_specs, check_vma=False)
```

```python
import jax
import jax.numpy as jnp
from jax import lax
from jax.sharding import PartitionSpec as P

slot_count = 2


def exact_parts(values):
    high = values.astype(jnp.bfloat16)
    rest = values - high.astype(jnp.float32)
    middle = rest.astype(jnp.bfloat16)
    low = (rest - middle.astype(jnp.float32)).astype(jnp.bfloat16)
    return jnp.concatenate([high, middle, low], axis=-1)


def rebuilt_slots(codebook_all, cell_codes):
    subspaces, sub_width, codewords = codebook_all.shape
    capacity = cell_codes.shape[1]
    parts = exact_parts(jnp.transpose(codebook_all, (0, 2, 1)))
    word_ids = jnp.arange(codewords, dtype=jnp.int32)
    one_hot = (cell_codes[:, :, None] == word_ids[None, None, :]).astype(jnp.bfloat16)
    picked = jnp.einsum("mvk,mkd->vmd", one_hot, parts, preferred_element_type=jnp.float32)
    rebuilt = (
        picked[..., :sub_width] + picked[..., sub_width : 2 * sub_width]
    ) + picked[..., 2 * sub_width :]
    return rebuilt.reshape(capacity, subspaces * sub_width)


def body(queries, probes, centroids, codebook, codes, cell_sizes):
    list_size = lax.axis_size("list")
    query_rows, probe_count = probes.shape
    cells_dev, subspaces, capacity = codes.shape
    dim = queries.shape[1]
    cell_count = cells_dev * list_size
    query_size = lax.axis_size("query")
    if query_size == 2:
        other = lax.ppermute(codebook, "query", [(0, 1), (1, 0)])
        first = lax.axis_index("query") == 0
        low_half = jnp.where(first, codebook, other)
        high_half = jnp.where(first, other, codebook)
        codebook_all = jnp.concatenate([low_half, high_half], axis=0)
    else:
        codebook_all = lax.all_gather(codebook, "query", axis=0, tiled=True)

    flat_cells = probes.reshape(-1)
    cell_ids = jnp.arange(cell_count, dtype=jnp.int32)
    contains = jnp.any(probes[:, :, None] == cell_ids[None, None, :], axis=1)
    counted = contains.astype(jnp.int32)
    earlier_rows = jnp.cumsum(counted, axis=0) - counted
    rank_of = jnp.take_along_axis(earlier_rows, probes, axis=1)
    slot_rank = rank_of.reshape(-1)
    lanes = 128
    tile_rows = dim // lanes
    query_tiles = queries.reshape(query_rows, tile_rows, lanes)
    row_at = jnp.full((cell_count, slot_count), -1, jnp.int32)
    for row in range(query_rows):
        here = contains[row][:, None] & (earlier_rows[row][:, None] == jnp.arange(slot_count)[None, :])
        row_at = jnp.where(here, row, row_at)
    selector = (row_at[:, :, None] == jnp.arange(query_rows)[None, None, :]).astype(jnp.float32)
    outgoing = jnp.einsum(
        "ckr,rij->ckij", selector, query_tiles, precision=lax.Precision.HIGHEST
    )
    outgoing = outgoing.reshape(list_size, cells_dev, slot_count, tile_rows, lanes)
    arrived = lax.all_to_all(outgoing, "list", split_axis=0, concat_axis=0, tiled=True)

    first_cell = lax.axis_index("list") * cells_dev
    positions = jnp.arange(capacity, dtype=jnp.int32)
    scored = []
    for local in range(cells_dev):
        centroid = lax.dynamic_slice_in_dim(centroids, first_cell + local, 1, axis=0)
        residual = arrived[:, local] - centroid.reshape(1, 1, tile_rows, lanes)
        own_norm = jnp.sum(residual * residual, axis=(2, 3)).reshape(-1)
        residual = residual.reshape(list_size * slot_count, dim)
        rebuilt = rebuilt_slots(codebook_all, codes[local])
        slot_norm = jnp.sum(rebuilt * rebuilt, axis=1)
        cross = jnp.einsum(
            "sf,vf->sv", residual, rebuilt, precision=lax.Precision.HIGH
        )
        total = (own_norm[:, None] + slot_norm[None, :]) - 2.0 * cross
        valid = positions < cell_sizes[local]
        total = jnp.where(valid[None, :], total, jnp.zeros((), jnp.float32))
        scored.append(total.reshape(list_size, slot_count, capacity))
    scored = jnp.stack(scored, axis=1)
    returned = lax.all_to_all(scored, "list", split_axis=0, concat_axis=0, tiled=True)
    returned = returned.reshape(cell_count * slot_count, capacity)
    result = returned[flat_cells * slot_count + slot_rank]
    return result.reshape(query_rows, probe_count, capacity)


def solution(mesh):
    in_specs = (
        P(("query", "list"), None),
        P(("query", "list"), None),
        P(),
        P("query", None, None),
        P("list", None, None),
        P("list"),
    )
    out_specs = P(("query", "list"), None, None)
    return jax.shard_map(body, mesh=mesh, in_specs=in_specs, out_specs=out_specs, check_vma=False)
```

```python
import jax
import jax.numpy as jnp
from jax import lax
from jax.sharding import PartitionSpec as P

slot_count = 2


def exact_parts(values):
    high = values.astype(jnp.bfloat16)
    rest = values - high.astype(jnp.float32)
    middle = rest.astype(jnp.bfloat16)
    low = (rest - middle.astype(jnp.float32)).astype(jnp.bfloat16)
    return jnp.concatenate([high, middle, low], axis=-1)


def rebuilt_slots(codebook_all, cell_codes):
    subspaces, sub_width, codewords = codebook_all.shape
    capacity = cell_codes.shape[1]
    parts = exact_parts(jnp.transpose(codebook_all, (0, 2, 1)))
    word_ids = jnp.arange(codewords, dtype=jnp.int32)
    one_hot = (cell_codes[:, :, None] == word_ids[None, None, :]).astype(jnp.bfloat16)
    picked = jnp.einsum("mvk,mkd->vmd", one_hot, parts, preferred_element_type=jnp.float32)
    rebuilt = (
        picked[..., :sub_width] + picked[..., sub_width : 2 * sub_width]
    ) + picked[..., 2 * sub_width :]
    return rebuilt.reshape(capacity, subspaces * sub_width)


def body(queries, probes, centroids, codebook, codes, cell_sizes):
    list_size = lax.axis_size("list")
    query_rows, probe_count = probes.shape
    cells_dev, subspaces, capacity = codes.shape
    dim = queries.shape[1]
    cell_count = cells_dev * list_size
    query_size = lax.axis_size("query")
    if query_size == 2:
        other = lax.ppermute(codebook, "query", [(0, 1), (1, 0)])
        first = lax.axis_index("query") == 0
        low_half = jnp.where(first, codebook, other)
        high_half = jnp.where(first, other, codebook)
        codebook_all = jnp.concatenate([low_half, high_half], axis=0)
    else:
        codebook_all = lax.all_gather(codebook, "query", axis=0, tiled=True)

    flat_cells = probes.reshape(-1)
    cell_ids = jnp.arange(cell_count, dtype=jnp.int32)
    contains = jnp.any(probes[:, :, None] == cell_ids[None, None, :], axis=1)
    counted = contains.astype(jnp.int32)
    earlier_rows = jnp.cumsum(counted, axis=0) - counted
    rank_of = jnp.take_along_axis(earlier_rows, probes, axis=1)
    slot_rank = rank_of.reshape(-1)
    lanes = 128
    tile_rows = dim // lanes
    query_tiles = queries.reshape(query_rows, tile_rows, lanes)
    row_at = jnp.full((cell_count, slot_count), -1, jnp.int32)
    for row in range(query_rows):
        here = contains[row][:, None] & (earlier_rows[row][:, None] == jnp.arange(slot_count)[None, :])
        row_at = jnp.where(here, row, row_at)
    tile_table = jnp.concatenate(
        [query_tiles, jnp.zeros((1, tile_rows, lanes), jnp.float32)], axis=0
    )
    outgoing = tile_table[jnp.where(row_at >= 0, row_at, query_rows)]
    outgoing = outgoing.reshape(list_size, cells_dev, slot_count, tile_rows, lanes)
    arrived = lax.all_to_all(outgoing, "list", split_axis=0, concat_axis=0, tiled=True)

    first_cell = lax.axis_index("list") * cells_dev
    positions = jnp.arange(capacity, dtype=jnp.int32)
    scored = []
    for local in range(cells_dev):
        centroid = lax.dynamic_slice_in_dim(centroids, first_cell + local, 1, axis=0)
        residual = arrived[:, local] - centroid.reshape(1, 1, tile_rows, lanes)
        own_norm = jnp.sum(residual * residual, axis=(2, 3)).reshape(-1)
        residual = residual.reshape(list_size * slot_count, dim)
        rebuilt = rebuilt_slots(codebook_all, codes[local])
        slot_norm = jnp.sum(rebuilt * rebuilt, axis=1)
        cross = jnp.einsum(
            "sf,vf->sv", residual, rebuilt, precision=lax.Precision.HIGH
        )
        total = (own_norm[:, None] + slot_norm[None, :]) - 2.0 * cross
        valid = positions < cell_sizes[local]
        total = jnp.where(valid[None, :], total, jnp.zeros((), jnp.float32))
        scored.append(total.reshape(list_size, slot_count, capacity))
    scored = jnp.stack(scored, axis=1)
    returned = lax.all_to_all(scored, "list", split_axis=0, concat_axis=0, tiled=True)
    returned = returned.reshape(cell_count * slot_count, capacity)
    result = returned[flat_cells * slot_count + slot_rank]
    return result.reshape(query_rows, probe_count, capacity)


def solution(mesh):
    in_specs = (
        P(("query", "list"), None),
        P(("query", "list"), None),
        P(),
        P("query", None, None),
        P("list", None, None),
        P("list"),
    )
    out_specs = P(("query", "list"), None, None)
    return jax.shard_map(body, mesh=mesh, in_specs=in_specs, out_specs=out_specs, check_vma=False)
```

```python
import jax
import jax.numpy as jnp
from jax import lax
from jax.sharding import PartitionSpec as P

slot_count = 2


def exact_parts(values):
    high = values.astype(jnp.bfloat16)
    rest = values - high.astype(jnp.float32)
    middle = rest.astype(jnp.bfloat16)
    low = (rest - middle.astype(jnp.float32)).astype(jnp.bfloat16)
    return jnp.concatenate([high, middle, low], axis=-1)


def rebuilt_slots(codebook_all, cell_codes):
    subspaces, sub_width, codewords = codebook_all.shape
    capacity = cell_codes.shape[1]
    parts = exact_parts(jnp.transpose(codebook_all, (0, 2, 1)))
    word_ids = jnp.arange(codewords, dtype=jnp.int32)
    one_hot = (cell_codes[:, :, None] == word_ids[None, None, :]).astype(jnp.bfloat16)
    picked = jnp.einsum("mvk,mkd->vmd", one_hot, parts, preferred_element_type=jnp.float32)
    rebuilt = (
        picked[..., :sub_width] + picked[..., sub_width : 2 * sub_width]
    ) + picked[..., 2 * sub_width :]
    return rebuilt.reshape(capacity, subspaces * sub_width)


def body(queries, probes, centroids, codebook, codes, cell_sizes):
    list_size = lax.axis_size("list")
    query_rows, probe_count = probes.shape
    cells_dev, subspaces, capacity = codes.shape
    dim = queries.shape[1]
    cell_count = cells_dev * list_size
    query_size = lax.axis_size("query")
    if query_size == 2:
        other = lax.ppermute(codebook, "query", [(0, 1), (1, 0)])
        first = lax.axis_index("query") == 0
        low_half = jnp.where(first, codebook, other)
        high_half = jnp.where(first, other, codebook)
        codebook_all = jnp.concatenate([low_half, high_half], axis=0)
    else:
        codebook_all = lax.all_gather(codebook, "query", axis=0, tiled=True)

    flat_cells = probes.reshape(-1)
    cell_ids = jnp.arange(cell_count, dtype=jnp.int32)
    contains = jnp.any(probes[:, :, None] == cell_ids[None, None, :], axis=1)
    counted = contains.astype(jnp.int32)
    earlier_rows = jnp.cumsum(counted, axis=0) - counted
    rank_of = jnp.take_along_axis(earlier_rows, probes, axis=1)
    slot_rank = rank_of.reshape(-1)
    lanes = 128
    tile_rows = dim // lanes
    query_tiles = queries.reshape(query_rows, tile_rows, lanes)
    row_at = jnp.full((cell_count, slot_count), -1, jnp.int32)
    for row in range(query_rows):
        here = contains[row][:, None] & (earlier_rows[row][:, None] == jnp.arange(slot_count)[None, :])
        row_at = jnp.where(here, row, row_at)
    selector = (row_at[:, :, None] == jnp.arange(query_rows)[None, None, :]).astype(jnp.float32)
    outgoing = jnp.einsum(
        "ckr,rij->ckij", selector, query_tiles, precision=lax.Precision.HIGHEST
    )
    outgoing = outgoing.reshape(list_size, cells_dev, slot_count, tile_rows, lanes)
    arrived = lax.all_to_all(outgoing, "list", split_axis=0, concat_axis=0, tiled=True)

    first_cell = lax.axis_index("list") * cells_dev
    positions = jnp.arange(capacity, dtype=jnp.int32)
    scored = []
    for local in range(cells_dev):
        centroid = lax.dynamic_slice_in_dim(centroids, first_cell + local, 1, axis=0)
        residual = arrived[:, local] - centroid.reshape(1, 1, tile_rows, lanes)
        own_norm = jnp.sum(residual * residual, axis=(2, 3))
        rebuilt = rebuilt_slots(codebook_all, codes[local])
        slot_norm = jnp.sum(rebuilt * rebuilt, axis=1)
        cross = jnp.einsum(
            "skij,vij->skv", residual, rebuilt.reshape(capacity, tile_rows, lanes),
            precision=lax.Precision.HIGH,
        )
        total = (own_norm[:, :, None] + slot_norm[None, None, :]) - 2.0 * cross
        valid = positions < cell_sizes[local]
        total = jnp.where(valid[None, None, :], total, jnp.zeros((), jnp.float32))
        scored.append(total)
    scored = jnp.stack(scored, axis=1)
    returned = lax.all_to_all(scored, "list", split_axis=0, concat_axis=0, tiled=True)
    returned = returned.reshape(cell_count, slot_count, capacity)
    result = returned[flat_cells, slot_rank]
    return result.reshape(query_rows, probe_count, capacity)


def solution(mesh):
    in_specs = (
        P(("query", "list"), None),
        P(("query", "list"), None),
        P(),
        P("query", None, None),
        P("list", None, None),
        P("list"),
    )
    out_specs = P(("query", "list"), None, None)
    return jax.shard_map(body, mesh=mesh, in_specs=in_specs, out_specs=out_specs, check_vma=False)
```

```python
import jax
import jax.numpy as jnp
from jax import lax
from jax.sharding import PartitionSpec as P

slot_count = 2


def exact_parts(values):
    high = values.astype(jnp.bfloat16)
    rest = values - high.astype(jnp.float32)
    middle = rest.astype(jnp.bfloat16)
    low = (rest - middle.astype(jnp.float32)).astype(jnp.bfloat16)
    return jnp.concatenate([high, middle, low], axis=-1)


def rebuilt_slots(codebook_all, cell_codes):
    subspaces, sub_width, codewords = codebook_all.shape
    capacity = cell_codes.shape[1]
    word_norm = jnp.sum(codebook_all * codebook_all, axis=1)
    columns = jnp.concatenate(
        [jnp.transpose(codebook_all, (0, 2, 1)), word_norm[:, :, None]], axis=-1
    )
    parts = exact_parts(columns)
    width = sub_width + 1
    word_ids = jnp.arange(codewords, dtype=jnp.int32)
    one_hot = (cell_codes[:, :, None] == word_ids[None, None, :]).astype(jnp.bfloat16)
    picked = jnp.einsum("mvk,mkd->vmd", one_hot, parts, preferred_element_type=jnp.float32)
    joined = (picked[..., :width] + picked[..., width : 2 * width]) + picked[..., 2 * width :]
    rebuilt = joined[..., :sub_width].reshape(capacity, subspaces * sub_width)
    slot_norm = jnp.sum(joined[..., sub_width], axis=1)
    return rebuilt, slot_norm


def body(queries, probes, centroids, codebook, codes, cell_sizes):
    list_size = lax.axis_size("list")
    query_rows, probe_count = probes.shape
    cells_dev, subspaces, capacity = codes.shape
    dim = queries.shape[1]
    cell_count = cells_dev * list_size
    query_size = lax.axis_size("query")
    if query_size == 2:
        other = lax.ppermute(codebook, "query", [(0, 1), (1, 0)])
        first = lax.axis_index("query") == 0
        low_half = jnp.where(first, codebook, other)
        high_half = jnp.where(first, other, codebook)
        codebook_all = jnp.concatenate([low_half, high_half], axis=0)
    else:
        codebook_all = lax.all_gather(codebook, "query", axis=0, tiled=True)

    flat_cells = probes.reshape(-1)
    cell_ids = jnp.arange(cell_count, dtype=jnp.int32)
    contains = jnp.any(probes[:, :, None] == cell_ids[None, None, :], axis=1)
    counted = contains.astype(jnp.int32)
    earlier_rows = jnp.cumsum(counted, axis=0) - counted
    rank_of = jnp.take_along_axis(earlier_rows, probes, axis=1)
    slot_rank = rank_of.reshape(-1)
    lanes = 128
    tile_rows = dim // lanes
    query_tiles = queries.reshape(query_rows, tile_rows, lanes)
    row_at = jnp.full((cell_count, slot_count), -1, jnp.int32)
    for row in range(query_rows):
        here = contains[row][:, None] & (earlier_rows[row][:, None] == jnp.arange(slot_count)[None, :])
        row_at = jnp.where(here, row, row_at)
    selector = (row_at[:, :, None] == jnp.arange(query_rows)[None, None, :]).astype(jnp.float32)
    outgoing = jnp.einsum(
        "ckr,rij->ckij", selector, query_tiles, precision=lax.Precision.HIGHEST
    )
    outgoing = outgoing.reshape(list_size, cells_dev, slot_count, tile_rows, lanes)
    arrived = lax.all_to_all(outgoing, "list", split_axis=0, concat_axis=0, tiled=True)

    first_cell = lax.axis_index("list") * cells_dev
    positions = jnp.arange(capacity, dtype=jnp.int32)
    scored = []
    for local in range(cells_dev):
        centroid = lax.dynamic_slice_in_dim(centroids, first_cell + local, 1, axis=0)
        residual = arrived[:, local] - centroid.reshape(1, 1, tile_rows, lanes)
        own_norm = jnp.sum(residual * residual, axis=(2, 3)).reshape(-1)
        residual = residual.reshape(list_size * slot_count, dim)
        rebuilt, slot_norm = rebuilt_slots(codebook_all, codes[local])
        cross = jnp.einsum(
            "sf,vf->sv", residual, rebuilt, precision=lax.Precision.HIGH
        )
        total = (own_norm[:, None] + slot_norm[None, :]) - 2.0 * cross
        valid = positions < cell_sizes[local]
        total = jnp.where(valid[None, :], total, jnp.zeros((), jnp.float32))
        scored.append(total.reshape(list_size, slot_count, capacity))
    scored = jnp.stack(scored, axis=1)
    returned = lax.all_to_all(scored, "list", split_axis=0, concat_axis=0, tiled=True)
    returned = returned.reshape(cell_count * slot_count, capacity)
    result = returned[flat_cells * slot_count + slot_rank]
    return result.reshape(query_rows, probe_count, capacity)


def solution(mesh):
    in_specs = (
        P(("query", "list"), None),
        P(("query", "list"), None),
        P(),
        P("query", None, None),
        P("list", None, None),
        P("list"),
    )
    out_specs = P(("query", "list"), None, None)
    return jax.shard_map(body, mesh=mesh, in_specs=in_specs, out_specs=out_specs, check_vma=False)
```

```python
import jax
import jax.numpy as jnp
from jax import lax
from jax.sharding import PartitionSpec as P

slot_count = 2


def exact_parts(values):
    high = values.astype(jnp.bfloat16)
    rest = values - high.astype(jnp.float32)
    middle = rest.astype(jnp.bfloat16)
    low = (rest - middle.astype(jnp.float32)).astype(jnp.bfloat16)
    return jnp.concatenate([high, middle, low], axis=-1)


def rebuilt_slots(codebook_all, cell_codes):
    subspaces, sub_width, codewords = codebook_all.shape
    capacity = cell_codes.shape[1]
    parts = exact_parts(jnp.transpose(codebook_all, (0, 2, 1)))
    word_ids = jnp.arange(codewords, dtype=jnp.int32)
    one_hot = (cell_codes[:, :, None] == word_ids[None, None, :]).astype(jnp.bfloat16)
    picked = jnp.einsum("mvk,mkd->vmd", one_hot, parts, preferred_element_type=jnp.float32)
    rebuilt = (
        picked[..., :sub_width] + picked[..., sub_width : 2 * sub_width]
    ) + picked[..., 2 * sub_width :]
    return rebuilt.reshape(capacity, subspaces * sub_width)


def body(queries, probes, centroids, codebook, codes, cell_sizes):
    list_size = lax.axis_size("list")
    query_rows, probe_count = probes.shape
    cells_dev, subspaces, capacity = codes.shape
    dim = queries.shape[1]
    cell_count = cells_dev * list_size
    query_size = lax.axis_size("query")
    if query_size == 2:
        other = lax.ppermute(codebook, "query", [(0, 1), (1, 0)])
        first = lax.axis_index("query") == 0
        low_half = jnp.where(first, codebook, other)
        high_half = jnp.where(first, other, codebook)
        codebook_all = jnp.concatenate([low_half, high_half], axis=0)
    else:
        codebook_all = lax.all_gather(codebook, "query", axis=0, tiled=True)

    flat_cells = probes.reshape(-1)
    cell_ids = jnp.arange(cell_count, dtype=jnp.int32)
    contains = jnp.any(probes[:, :, None] == cell_ids[None, None, :], axis=1)
    counted = contains.astype(jnp.int32)
    earlier_rows = jnp.cumsum(counted, axis=0) - counted
    rank_of = jnp.take_along_axis(earlier_rows, probes, axis=1)
    slot_rank = rank_of.reshape(-1)
    lanes = 128
    tile_rows = dim // lanes
    query_tiles = queries.reshape(query_rows, tile_rows, lanes)
    row_at = jnp.full((cell_count, slot_count), -1, jnp.int32)
    for row in range(query_rows):
        here = contains[row][:, None] & (earlier_rows[row][:, None] == jnp.arange(slot_count)[None, :])
        row_at = jnp.where(here, row, row_at)
    selector = (row_at[:, :, None] == jnp.arange(query_rows)[None, None, :]).astype(jnp.float32)
    outgoing = jnp.einsum(
        "ckr,rij->ckij", selector, query_tiles, precision=lax.Precision.HIGHEST
    )
    outgoing = outgoing.reshape(list_size, cells_dev, slot_count, tile_rows, lanes)
    arrived = lax.all_to_all(outgoing, "list", split_axis=0, concat_axis=0, tiled=True)

    first_cell = lax.axis_index("list") * cells_dev
    positions = jnp.arange(capacity, dtype=jnp.int32)
    scored = []
    for local in range(cells_dev):
        centroid = lax.dynamic_slice_in_dim(centroids, first_cell + local, 1, axis=0)
        residual = arrived[:, local] - centroid.reshape(1, 1, tile_rows, lanes)
        own_norm = jnp.sum(residual * residual, axis=(2, 3)).reshape(-1)
        residual = residual.reshape(list_size * slot_count, dim)
        rebuilt = rebuilt_slots(codebook_all, codes[local])
        slot_norm = jnp.sum(rebuilt * rebuilt, axis=1)
        half = capacity // 2
        cross = jnp.concatenate(
            [
                jnp.einsum(
                    "sf,vf->sv", residual, rebuilt[part * half : (part + 1) * half],
                    precision=lax.Precision.HIGH,
                )
                for part in range(2)
            ],
            axis=1,
        )
        total = (own_norm[:, None] + slot_norm[None, :]) - 2.0 * cross
        valid = positions < cell_sizes[local]
        total = jnp.where(valid[None, :], total, jnp.zeros((), jnp.float32))
        scored.append(total.reshape(list_size, slot_count, capacity))
    scored = jnp.stack(scored, axis=1)
    returned = lax.all_to_all(scored, "list", split_axis=0, concat_axis=0, tiled=True)
    returned = returned.reshape(cell_count, slot_count, capacity)
    result = returned[flat_cells, slot_rank]
    return result.reshape(query_rows, probe_count, capacity)


def solution(mesh):
    in_specs = (
        P(("query", "list"), None),
        P(("query", "list"), None),
        P(),
        P("query", None, None),
        P("list", None, None),
        P("list"),
    )
    out_specs = P(("query", "list"), None, None)
    return jax.shard_map(body, mesh=mesh, in_specs=in_specs, out_specs=out_specs, check_vma=False)
```

```python
import jax
import jax.numpy as jnp
from jax import lax
from jax.sharding import PartitionSpec as P

slot_count = 2


def exact_parts(values):
    high = values.astype(jnp.bfloat16)
    rest = values - high.astype(jnp.float32)
    middle = rest.astype(jnp.bfloat16)
    low = (rest - middle.astype(jnp.float32)).astype(jnp.bfloat16)
    return jnp.concatenate([high, middle, low], axis=-1)


def rebuilt_slots(codebook_all, cell_codes):
    subspaces, sub_width, codewords = codebook_all.shape
    capacity = cell_codes.shape[1]
    parts = exact_parts(jnp.transpose(codebook_all, (0, 2, 1)))
    word_ids = jnp.arange(codewords, dtype=jnp.int32)
    one_hot = (cell_codes[:, :, None] == word_ids[None, None, :]).astype(jnp.bfloat16)
    picked = jnp.einsum("mvk,mkd->vmd", one_hot, parts, preferred_element_type=jnp.float32)
    rebuilt = (
        picked[..., :sub_width] + picked[..., sub_width : 2 * sub_width]
    ) + picked[..., 2 * sub_width :]
    return rebuilt.reshape(capacity, subspaces * sub_width)


def body(queries, probes, centroids, codebook, codes, cell_sizes):
    list_size = lax.axis_size("list")
    query_rows, probe_count = probes.shape
    cells_dev, subspaces, capacity = codes.shape
    dim = queries.shape[1]
    cell_count = cells_dev * list_size
    query_size = lax.axis_size("query")
    if query_size == 2:
        other = lax.ppermute(codebook, "query", [(0, 1), (1, 0)])
        first = lax.axis_index("query") == 0
        low_half = jnp.where(first, codebook, other)
        high_half = jnp.where(first, other, codebook)
        codebook_all = jnp.concatenate([low_half, high_half], axis=0)
    else:
        codebook_all = lax.all_gather(codebook, "query", axis=0, tiled=True)

    flat_cells = probes.reshape(-1)
    cell_ids = jnp.arange(cell_count, dtype=jnp.int32)
    contains = jnp.any(probes[:, :, None] == cell_ids[None, None, :], axis=1)
    counted = contains.astype(jnp.int32)
    earlier_rows = jnp.cumsum(counted, axis=0) - counted
    rank_of = jnp.take_along_axis(earlier_rows, probes, axis=1)
    slot_rank = rank_of.reshape(-1)
    lanes = 128
    tile_rows = dim // lanes
    query_tiles = queries.reshape(query_rows, tile_rows, lanes)
    row_at = jnp.full((cell_count, slot_count), -1, jnp.int32)
    for row in range(query_rows):
        here = contains[row][:, None] & (earlier_rows[row][:, None] == jnp.arange(slot_count)[None, :])
        row_at = jnp.where(here, row, row_at)
    selector = (row_at[:, :, None] == jnp.arange(query_rows)[None, None, :]).astype(jnp.bfloat16)
    selector = jnp.concatenate([selector] * 3, axis=-1)
    query_parts = exact_parts(queries.reshape(query_rows, 1, dim))
    query_parts = jnp.transpose(query_parts.reshape(query_rows, 3, dim), (1, 0, 2))
    query_parts = query_parts.reshape(3 * query_rows, tile_rows, lanes)
    outgoing = jnp.einsum(
        "ckr,rij->ckij", selector, query_parts, preferred_element_type=jnp.float32
    )
    outgoing = outgoing.reshape(list_size, cells_dev, slot_count, tile_rows, lanes)
    arrived = lax.all_to_all(outgoing, "list", split_axis=0, concat_axis=0, tiled=True)

    first_cell = lax.axis_index("list") * cells_dev
    positions = jnp.arange(capacity, dtype=jnp.int32)
    scored = []
    for local in range(cells_dev):
        centroid = lax.dynamic_slice_in_dim(centroids, first_cell + local, 1, axis=0)
        residual = arrived[:, local] - centroid.reshape(1, 1, tile_rows, lanes)
        own_norm = jnp.sum(residual * residual, axis=(2, 3)).reshape(-1)
        residual = residual.reshape(list_size * slot_count, dim)
        rebuilt = rebuilt_slots(codebook_all, codes[local])
        slot_norm = jnp.sum(rebuilt * rebuilt, axis=1)
        cross = jnp.einsum(
            "sf,vf->sv", residual, rebuilt, precision=lax.Precision.HIGH
        )
        total = (own_norm[:, None] + slot_norm[None, :]) - 2.0 * cross
        valid = positions < cell_sizes[local]
        total = jnp.where(valid[None, :], total, jnp.zeros((), jnp.float32))
        scored.append(total.reshape(list_size, slot_count, capacity))
    scored = jnp.stack(scored, axis=1)
    returned = lax.all_to_all(scored, "list", split_axis=0, concat_axis=0, tiled=True)
    returned = returned.reshape(cell_count * slot_count, capacity)
    result = returned[flat_cells * slot_count + slot_rank]
    return result.reshape(query_rows, probe_count, capacity)


def solution(mesh):
    in_specs = (
        P(("query", "list"), None),
        P(("query", "list"), None),
        P(),
        P("query", None, None),
        P("list", None, None),
        P("list"),
    )
    out_specs = P(("query", "list"), None, None)
    return jax.shard_map(body, mesh=mesh, in_specs=in_specs, out_specs=out_specs, check_vma=False)
```

```python
import jax
import jax.numpy as jnp
from jax import lax
from jax.sharding import PartitionSpec as P

slot_count = 2


def exact_parts(values):
    high = lax.reduce_precision(values, exponent_bits=8, mantissa_bits=7)
    rest = values - high
    middle = lax.reduce_precision(rest, exponent_bits=8, mantissa_bits=7)
    low = rest - middle
    return jnp.concatenate([high, middle, low], axis=-1).astype(jnp.bfloat16)


def rebuilt_slots(codebook_all, cell_codes):
    subspaces, sub_width, codewords = codebook_all.shape
    capacity = cell_codes.shape[1]
    parts = exact_parts(jnp.transpose(codebook_all, (0, 2, 1)))
    word_ids = jnp.arange(codewords, dtype=jnp.int32)
    one_hot = (cell_codes[:, :, None] == word_ids[None, None, :]).astype(jnp.bfloat16)
    picked = jnp.einsum("mvk,mkd->vmd", one_hot, parts, preferred_element_type=jnp.float32)
    rebuilt = (
        picked[..., :sub_width] + picked[..., sub_width : 2 * sub_width]
    ) + picked[..., 2 * sub_width :]
    return rebuilt.reshape(capacity, subspaces * sub_width)


def body(queries, probes, centroids, codebook, codes, cell_sizes):
    list_size = lax.axis_size("list")
    query_rows, probe_count = probes.shape
    cells_dev, subspaces, capacity = codes.shape
    dim = queries.shape[1]
    cell_count = cells_dev * list_size
    query_size = lax.axis_size("query")
    if query_size == 2:
        other = lax.ppermute(codebook, "query", [(0, 1), (1, 0)])
        first = lax.axis_index("query") == 0
        low_half = jnp.where(first, codebook, other)
        high_half = jnp.where(first, other, codebook)
        codebook_all = jnp.concatenate([low_half, high_half], axis=0)
    else:
        codebook_all = lax.all_gather(codebook, "query", axis=0, tiled=True)

    flat_cells = probes.reshape(-1)
    cell_ids = jnp.arange(cell_count, dtype=jnp.int32)
    contains = jnp.any(probes[:, :, None] == cell_ids[None, None, :], axis=1)
    counted = contains.astype(jnp.int32)
    earlier_rows = jnp.cumsum(counted, axis=0) - counted
    rank_of = jnp.take_along_axis(earlier_rows, probes, axis=1)
    slot_rank = rank_of.reshape(-1)
    lanes = 128
    tile_rows = dim // lanes
    query_tiles = queries.reshape(query_rows, tile_rows, lanes)
    row_at = jnp.full((cell_count, slot_count), -1, jnp.int32)
    for row in range(query_rows):
        here = contains[row][:, None] & (earlier_rows[row][:, None] == jnp.arange(slot_count)[None, :])
        row_at = jnp.where(here, row, row_at)
    selector = (row_at[:, :, None] == jnp.arange(query_rows)[None, None, :]).astype(jnp.bfloat16)
    selector = jnp.concatenate([selector] * 3, axis=-1)
    query_parts = exact_parts(queries.reshape(query_rows, 1, dim))
    query_parts = jnp.transpose(query_parts.reshape(query_rows, 3, dim), (1, 0, 2))
    query_parts = query_parts.reshape(3 * query_rows, tile_rows, lanes)
    outgoing = jnp.einsum(
        "ckr,rij->ckij", selector, query_parts, preferred_element_type=jnp.float32
    )
    outgoing = outgoing.reshape(list_size, cells_dev, slot_count, tile_rows, lanes)
    arrived = lax.all_to_all(outgoing, "list", split_axis=0, concat_axis=0, tiled=True)

    first_cell = lax.axis_index("list") * cells_dev
    positions = jnp.arange(capacity, dtype=jnp.int32)
    scored = []
    for local in range(cells_dev):
        centroid = lax.dynamic_slice_in_dim(centroids, first_cell + local, 1, axis=0)
        residual = arrived[:, local] - centroid.reshape(1, 1, tile_rows, lanes)
        own_norm = jnp.sum(residual * residual, axis=(2, 3)).reshape(-1)
        residual = residual.reshape(list_size * slot_count, dim)
        rebuilt = rebuilt_slots(codebook_all, codes[local])
        slot_norm = jnp.sum(rebuilt * rebuilt, axis=1)
        cross = jnp.einsum(
            "sf,vf->sv", residual, rebuilt, precision=lax.Precision.HIGH
        )
        total = (own_norm[:, None] + slot_norm[None, :]) - 2.0 * cross
        valid = positions < cell_sizes[local]
        total = jnp.where(valid[None, :], total, jnp.zeros((), jnp.float32))
        scored.append(total.reshape(list_size, slot_count, capacity))
    scored = jnp.stack(scored, axis=1)
    returned = lax.all_to_all(scored, "list", split_axis=0, concat_axis=0, tiled=True)
    returned = returned.reshape(cell_count * slot_count, capacity)
    result = returned[flat_cells * slot_count + slot_rank]
    return result.reshape(query_rows, probe_count, capacity)


def solution(mesh):
    in_specs = (
        P(("query", "list"), None),
        P(("query", "list"), None),
        P(),
        P("query", None, None),
        P("list", None, None),
        P("list"),
    )
    out_specs = P(("query", "list"), None, None)
    return jax.shard_map(body, mesh=mesh, in_specs=in_specs, out_specs=out_specs, check_vma=False)
```

```python
import jax
import jax.numpy as jnp
from jax import lax
from jax.sharding import PartitionSpec as P

slot_count = 2


def exact_parts(values):
    high = lax.reduce_precision(values, exponent_bits=8, mantissa_bits=7)
    rest = values - high
    middle = lax.reduce_precision(rest, exponent_bits=8, mantissa_bits=7)
    low = rest - middle
    return jnp.concatenate([high, middle, low], axis=-1).astype(jnp.bfloat16)


def rebuilt_slots(codebook_all, cell_codes):
    subspaces, sub_width, codewords = codebook_all.shape
    capacity = cell_codes.shape[1]
    parts = exact_parts(jnp.transpose(codebook_all, (0, 2, 1)))
    word_ids = jnp.arange(codewords, dtype=jnp.int32)
    one_hot = (cell_codes[:, :, None] == word_ids[None, None, :]).astype(jnp.bfloat16)
    picked = jnp.einsum("mvk,mkd->vmd", one_hot, parts, preferred_element_type=jnp.float32)
    rebuilt = (
        picked[..., :sub_width] + picked[..., sub_width : 2 * sub_width]
    ) + picked[..., 2 * sub_width :]
    return rebuilt.reshape(capacity, subspaces * sub_width)


def body(queries, probes, centroids, codebook, codes, cell_sizes):
    list_size = lax.axis_size("list")
    query_rows, probe_count = probes.shape
    cells_dev, subspaces, capacity = codes.shape
    dim = queries.shape[1]
    cell_count = cells_dev * list_size
    query_size = lax.axis_size("query")
    if query_size == 2:
        other = lax.ppermute(codebook, "query", [(0, 1), (1, 0)])
        first = lax.axis_index("query") == 0
        low_half = jnp.where(first, codebook, other)
        high_half = jnp.where(first, other, codebook)
        codebook_all = jnp.concatenate([low_half, high_half], axis=0)
    else:
        codebook_all = lax.all_gather(codebook, "query", axis=0, tiled=True)

    flat_cells = probes.reshape(-1)
    cell_ids = jnp.arange(cell_count, dtype=jnp.int32)
    probe_hot = (flat_cells[:, None] == cell_ids[None, :]).astype(jnp.bfloat16)
    row_of = jnp.arange(query_rows * probe_count, dtype=jnp.int32) // probe_count
    row_hot = (jnp.arange(query_rows)[:, None] == row_of[None, :]).astype(jnp.bfloat16)
    counted = jnp.einsum(
        "rp,pc->rc", row_hot, probe_hot, preferred_element_type=jnp.float32
    ).astype(jnp.int32)
    contains = counted > 0
    earlier_rows = jnp.cumsum(counted, axis=0) - counted
    rank_of = jnp.take_along_axis(earlier_rows, probes, axis=1)
    slot_rank = rank_of.reshape(-1)
    lanes = 128
    tile_rows = dim // lanes
    query_tiles = queries.reshape(query_rows, tile_rows, lanes)
    row_at = jnp.full((cell_count, slot_count), -1, jnp.int32)
    for row in range(query_rows):
        here = contains[row][:, None] & (earlier_rows[row][:, None] == jnp.arange(slot_count)[None, :])
        row_at = jnp.where(here, row, row_at)
    selector = (row_at[:, :, None] == jnp.arange(query_rows)[None, None, :]).astype(jnp.bfloat16)
    selector = jnp.concatenate([selector] * 3, axis=-1)
    query_parts = exact_parts(queries.reshape(query_rows, 1, dim))
    query_parts = jnp.transpose(query_parts.reshape(query_rows, 3, dim), (1, 0, 2))
    query_parts = query_parts.reshape(3 * query_rows, tile_rows, lanes)
    outgoing = jnp.einsum(
        "ckr,rij->ckij", selector, query_parts, preferred_element_type=jnp.float32
    )
    outgoing = outgoing.reshape(list_size, cells_dev, slot_count, tile_rows, lanes)
    arrived = lax.all_to_all(outgoing, "list", split_axis=0, concat_axis=0, tiled=True)

    first_cell = lax.axis_index("list") * cells_dev
    positions = jnp.arange(capacity, dtype=jnp.int32)
    scored = []
    for local in range(cells_dev):
        centroid = lax.dynamic_slice_in_dim(centroids, first_cell + local, 1, axis=0)
        residual = arrived[:, local] - centroid.reshape(1, 1, tile_rows, lanes)
        own_norm = jnp.sum(residual * residual, axis=(2, 3)).reshape(-1)
        residual = residual.reshape(list_size * slot_count, dim)
        rebuilt = rebuilt_slots(codebook_all, codes[local])
        slot_norm = jnp.sum(rebuilt * rebuilt, axis=1)
        cross = jnp.einsum(
            "sf,vf->sv", residual, rebuilt, precision=lax.Precision.HIGH
        )
        total = (own_norm[:, None] + slot_norm[None, :]) - 2.0 * cross
        valid = positions < cell_sizes[local]
        total = jnp.where(valid[None, :], total, jnp.zeros((), jnp.float32))
        scored.append(total.reshape(list_size, slot_count, capacity))
    scored = jnp.stack(scored, axis=1)
    returned = lax.all_to_all(scored, "list", split_axis=0, concat_axis=0, tiled=True)
    returned = returned.reshape(cell_count * slot_count, capacity)
    result = returned[flat_cells * slot_count + slot_rank]
    return result.reshape(query_rows, probe_count, capacity)


def solution(mesh):
    in_specs = (
        P(("query", "list"), None),
        P(("query", "list"), None),
        P(),
        P("query", None, None),
        P("list", None, None),
        P("list"),
    )
    out_specs = P(("query", "list"), None, None)
    return jax.shard_map(body, mesh=mesh, in_specs=in_specs, out_specs=out_specs, check_vma=False)
```

```python
import jax
import jax.numpy as jnp
from jax import lax
from jax.sharding import PartitionSpec as P

slot_count = 2


def exact_parts(values):
    high = lax.reduce_precision(values, exponent_bits=8, mantissa_bits=7)
    rest = values - high
    middle = lax.reduce_precision(rest, exponent_bits=8, mantissa_bits=7)
    low = rest - middle
    return jnp.concatenate([high, middle, low], axis=-1).astype(jnp.bfloat16)


def rebuilt_slots(codebook_all, cell_codes):
    subspaces, sub_width, codewords = codebook_all.shape
    capacity = cell_codes.shape[1]
    parts = exact_parts(jnp.transpose(codebook_all, (0, 2, 1)))
    word_ids = jnp.arange(codewords, dtype=jnp.int32)
    one_hot = (cell_codes[:, :, None] == word_ids[None, None, :]).astype(jnp.bfloat16)
    picked = jnp.einsum("mvk,mkd->vmd", one_hot, parts, preferred_element_type=jnp.float32)
    rebuilt = (
        picked[..., :sub_width] + picked[..., sub_width : 2 * sub_width]
    ) + picked[..., 2 * sub_width :]
    return rebuilt.reshape(capacity, subspaces * sub_width)


def body(queries, probes, centroids, codebook, codes, cell_sizes):
    list_size = lax.axis_size("list")
    query_rows, probe_count = probes.shape
    cells_dev, subspaces, capacity = codes.shape
    dim = queries.shape[1]
    cell_count = cells_dev * list_size
    query_size = lax.axis_size("query")
    if query_size == 2:
        other = lax.ppermute(codebook, "query", [(0, 1), (1, 0)])
        first = lax.axis_index("query") == 0
        low_half = jnp.where(first, codebook, other)
        high_half = jnp.where(first, other, codebook)
        codebook_all = jnp.concatenate([low_half, high_half], axis=0)
    else:
        codebook_all = lax.all_gather(codebook, "query", axis=0, tiled=True)

    flat_cells = probes.reshape(-1)
    cell_ids = jnp.arange(cell_count, dtype=jnp.int32)
    contains = jnp.any(probes[:, :, None] == cell_ids[None, None, :], axis=1)
    counted = contains.astype(jnp.int32)
    earlier_rows = jnp.cumsum(counted, axis=0) - counted
    rank_of = jnp.take_along_axis(earlier_rows, probes, axis=1)
    slot_rank = rank_of.reshape(-1)
    lanes = 128
    tile_rows = dim // lanes
    query_tiles = queries.reshape(query_rows, tile_rows, lanes)
    row_at = jnp.full((cell_count, slot_count), -1, jnp.int32)
    for row in range(query_rows):
        here = contains[row][:, None] & (earlier_rows[row][:, None] == jnp.arange(slot_count)[None, :])
        row_at = jnp.where(here, row, row_at)
    selector = (row_at[:, :, None] == jnp.arange(query_rows)[None, None, :]).astype(jnp.bfloat16)
    selector = jnp.concatenate([selector] * 3, axis=-1)
    query_parts = exact_parts(queries.reshape(query_rows, 1, dim))
    query_parts = jnp.transpose(query_parts.reshape(query_rows, 3, dim), (1, 0, 2))
    query_parts = query_parts.reshape(3 * query_rows, tile_rows, lanes)
    outgoing = jnp.einsum(
        "ckr,rij->ckij", selector, query_parts, preferred_element_type=jnp.float32
    )
    outgoing = outgoing.reshape(list_size, cells_dev, slot_count, tile_rows, lanes)
    arrived = lax.all_to_all(outgoing, "list", split_axis=0, concat_axis=0, tiled=True)

    first_cell = lax.axis_index("list") * cells_dev
    positions = jnp.arange(capacity, dtype=jnp.int32)
    scored = []
    for local in range(cells_dev):
        centroid = lax.dynamic_slice_in_dim(centroids, first_cell + local, 1, axis=0)
        residual = arrived[:, local] - centroid.reshape(1, 1, tile_rows, lanes)
        own_norm = jnp.sum(residual * residual, axis=(2, 3)).reshape(-1)
        residual = residual.reshape(list_size * slot_count, dim)
        rebuilt = rebuilt_slots(codebook_all, codes[local])
        slot_norm = jnp.sum(rebuilt * rebuilt, axis=1)
        cross = jnp.einsum(
            "sf,vf->sv", residual, rebuilt, precision=lax.Precision.HIGH
        )
        total = (own_norm[:, None] + slot_norm[None, :]) - 2.0 * cross
        valid = positions < cell_sizes[local]
        total = jnp.where(valid[None, :], total, jnp.zeros((), jnp.float32))
        scored.append(total.reshape(list_size, slot_count, capacity))
    scored = jnp.stack(scored, axis=1)
    returned = lax.all_to_all(scored, "list", split_axis=0, concat_axis=0, tiled=True)
    returned = returned.reshape(cell_count * slot_count, capacity)
    picks = flat_cells * slot_count + slot_rank
    pick_hot = (
        picks[:, None] == jnp.arange(cell_count * slot_count, dtype=jnp.int32)[None, :]
    ).astype(jnp.bfloat16)
    picked = jnp.einsum(
        "pr,rf->pf", pick_hot, exact_parts(returned), preferred_element_type=jnp.float32
    )
    result = (
        picked[:, :capacity] + picked[:, capacity : 2 * capacity]
    ) + picked[:, 2 * capacity :]
    return result.reshape(query_rows, probe_count, capacity)


def solution(mesh):
    in_specs = (
        P(("query", "list"), None),
        P(("query", "list"), None),
        P(),
        P("query", None, None),
        P("list", None, None),
        P("list"),
    )
    out_specs = P(("query", "list"), None, None)
    return jax.shard_map(body, mesh=mesh, in_specs=in_specs, out_specs=out_specs, check_vma=False)
```

```python
import jax
import jax.numpy as jnp
from jax import lax
from jax.sharding import PartitionSpec as P

slot_count = 2


def exact_parts(values):
    high = lax.reduce_precision(values, exponent_bits=8, mantissa_bits=7)
    rest = values - high
    middle = lax.reduce_precision(rest, exponent_bits=8, mantissa_bits=7)
    low = rest - middle
    return jnp.concatenate([high, middle, low], axis=-1).astype(jnp.bfloat16)


def rebuilt_slots(codebook_all, cell_codes):
    subspaces, sub_width, codewords = codebook_all.shape
    capacity = cell_codes.shape[1]
    parts = exact_parts(jnp.transpose(codebook_all, (0, 2, 1)))
    word_ids = jnp.arange(codewords, dtype=jnp.int32)
    one_hot = (cell_codes[:, :, None] == word_ids[None, None, :]).astype(jnp.bfloat16)
    picked = jnp.einsum("mvk,mkd->vmd", one_hot, parts, preferred_element_type=jnp.float32)
    rebuilt = (
        picked[..., :sub_width] + picked[..., sub_width : 2 * sub_width]
    ) + picked[..., 2 * sub_width :]
    return rebuilt.reshape(capacity, subspaces * sub_width)


def body(queries, probes, centroids, codebook, codes, cell_sizes):
    list_size = lax.axis_size("list")
    query_rows, probe_count = probes.shape
    cells_dev, subspaces, capacity = codes.shape
    dim = queries.shape[1]
    cell_count = cells_dev * list_size
    query_size = lax.axis_size("query")
    if query_size == 2:
        other = lax.ppermute(codebook, "query", [(0, 1), (1, 0)])
        first = lax.axis_index("query") == 0
        low_half = jnp.where(first, codebook, other)
        high_half = jnp.where(first, other, codebook)
        codebook_all = jnp.concatenate([low_half, high_half], axis=0)
    else:
        codebook_all = lax.all_gather(codebook, "query", axis=0, tiled=True)

    flat_cells = probes.reshape(-1)
    cell_ids = jnp.arange(cell_count, dtype=jnp.int32)
    contains = jnp.any(probes[:, :, None] == cell_ids[None, None, :], axis=1)
    counted = contains.astype(jnp.int32)
    earlier_rows = jnp.cumsum(counted, axis=0) - counted
    rank_of = jnp.take_along_axis(earlier_rows, probes, axis=1)
    slot_rank = rank_of.reshape(-1)
    lanes = 128
    tile_rows = dim // lanes
    query_tiles = queries.reshape(query_rows, tile_rows, lanes)
    row_at = jnp.full((cell_count, slot_count), -1, jnp.int32)
    for row in range(query_rows):
        here = contains[row][:, None] & (earlier_rows[row][:, None] == jnp.arange(slot_count)[None, :])
        row_at = jnp.where(here, row, row_at)
    selector = (row_at[:, :, None] == jnp.arange(query_rows)[None, None, :]).astype(jnp.bfloat16)
    selector = jnp.concatenate([selector] * 3, axis=-1)
    query_parts = exact_parts(queries.reshape(query_rows, 1, dim))
    query_parts = jnp.transpose(query_parts.reshape(query_rows, 3, dim), (1, 0, 2))
    query_parts = query_parts.reshape(3 * query_rows, tile_rows, lanes)
    outgoing = jnp.einsum(
        "ckr,rij->ckij", selector, query_parts, preferred_element_type=jnp.float32
    )
    outgoing = outgoing.reshape(list_size, cells_dev, slot_count, tile_rows, lanes)
    arrived = lax.all_to_all(outgoing, "list", split_axis=0, concat_axis=0, tiled=True)

    first_cell = lax.axis_index("list") * cells_dev
    positions = jnp.arange(capacity, dtype=jnp.int32)
    scored = []
    for local in range(cells_dev):
        centroid = lax.dynamic_slice_in_dim(centroids, first_cell + local, 1, axis=0)
        residual = arrived[:, local] - centroid.reshape(1, 1, tile_rows, lanes)
        own_norm = jnp.sum(residual * residual, axis=(2, 3)).reshape(-1)
        residual = residual.reshape(list_size * slot_count, dim)
        rebuilt = rebuilt_slots(codebook_all, codes[local])
        slot_norm = jnp.sum(rebuilt * rebuilt, axis=1)
        cross = jnp.einsum(
            "sf,vf->sv", residual, rebuilt, precision=lax.Precision.HIGH
        )
        total = (own_norm[:, None] + slot_norm[None, :]) - 2.0 * cross
        valid = positions < cell_sizes[local]
        total = jnp.where(valid[None, :], total, jnp.zeros((), jnp.float32))
        scored.append(total.reshape(list_size, slot_count, capacity // 128, 128))
    scored = jnp.stack(scored, axis=1)
    returned = lax.all_to_all(scored, "list", split_axis=0, concat_axis=0, tiled=True)
    returned = returned.reshape(cell_count * slot_count, capacity)
    picks = flat_cells * slot_count + slot_rank
    pick_hot = (
        picks[:, None] == jnp.arange(cell_count * slot_count, dtype=jnp.int32)[None, :]
    ).astype(jnp.bfloat16)
    picked = jnp.einsum(
        "pr,rf->pf", pick_hot, exact_parts(returned), preferred_element_type=jnp.float32
    )
    result = (
        picked[:, :capacity] + picked[:, capacity : 2 * capacity]
    ) + picked[:, 2 * capacity :]
    return result.reshape(query_rows, probe_count, capacity)


def solution(mesh):
    in_specs = (
        P(("query", "list"), None),
        P(("query", "list"), None),
        P(),
        P("query", None, None),
        P("list", None, None),
        P("list"),
    )
    out_specs = P(("query", "list"), None, None)
    return jax.shard_map(body, mesh=mesh, in_specs=in_specs, out_specs=out_specs, check_vma=False)
```

```python
import jax
import jax.numpy as jnp
from jax import lax
from jax.sharding import PartitionSpec as P

slot_count = 2


def exact_parts(values):
    high = lax.reduce_precision(values, exponent_bits=8, mantissa_bits=7)
    rest = values - high
    middle = lax.reduce_precision(rest, exponent_bits=8, mantissa_bits=7)
    low = rest - middle
    return jnp.concatenate([high, middle, low], axis=-1).astype(jnp.bfloat16)


def rebuilt_slots(codebook_all, cell_codes):
    subspaces, sub_width, codewords = codebook_all.shape
    capacity = cell_codes.shape[1]
    parts = exact_parts(jnp.transpose(codebook_all, (0, 2, 1)))
    word_ids = jnp.arange(codewords, dtype=jnp.int32)
    one_hot = (cell_codes[:, :, None] == word_ids[None, None, :]).astype(jnp.bfloat16)
    picked = jnp.einsum("mvk,mkd->vmd", one_hot, parts, preferred_element_type=jnp.float32)
    rebuilt = (
        picked[..., :sub_width] + picked[..., sub_width : 2 * sub_width]
    ) + picked[..., 2 * sub_width :]
    return rebuilt.reshape(capacity, subspaces * sub_width)


def body(queries, probes, centroids, codebook, codes, cell_sizes):
    list_size = lax.axis_size("list")
    query_rows, probe_count = probes.shape
    cells_dev, subspaces, capacity = codes.shape
    dim = queries.shape[1]
    cell_count = cells_dev * list_size
    query_size = lax.axis_size("query")
    if query_size == 2:
        other = lax.ppermute(codebook, "query", [(0, 1), (1, 0)])
        first = lax.axis_index("query") == 0
        low_half = jnp.where(first, codebook, other)
        high_half = jnp.where(first, other, codebook)
        codebook_all = jnp.concatenate([low_half, high_half], axis=0)
    else:
        codebook_all = lax.all_gather(codebook, "query", axis=0, tiled=True)

    flat_cells = probes.reshape(-1)
    cell_ids = jnp.arange(cell_count, dtype=jnp.int32)
    contains = jnp.any(probes[:, :, None] == cell_ids[None, None, :], axis=1)
    counted = contains.astype(jnp.int32)
    earlier_rows = jnp.cumsum(counted, axis=0) - counted
    rank_of = jnp.take_along_axis(earlier_rows, probes, axis=1)
    slot_rank = rank_of.reshape(-1)
    lanes = 128
    tile_rows = dim // lanes
    query_tiles = queries.reshape(query_rows, tile_rows, lanes)
    row_at = jnp.full((cell_count, slot_count), -1, jnp.int32)
    for row in range(query_rows):
        here = contains[row][:, None] & (earlier_rows[row][:, None] == jnp.arange(slot_count)[None, :])
        row_at = jnp.where(here, row, row_at)
    selector = (row_at[:, :, None] == jnp.arange(query_rows)[None, None, :]).astype(jnp.bfloat16)
    selector = jnp.concatenate([selector] * 3, axis=-1)
    query_parts = exact_parts(queries.reshape(query_rows, 1, dim))
    query_parts = jnp.transpose(query_parts.reshape(query_rows, 3, dim), (1, 0, 2))
    query_parts = query_parts.reshape(3 * query_rows, tile_rows, lanes)
    outgoing = jnp.einsum(
        "ckr,rij->ckij", selector, query_parts, preferred_element_type=jnp.float32
    )
    outgoing = outgoing.reshape(list_size, cells_dev, slot_count, tile_rows, lanes)
    arrived = lax.all_to_all(outgoing, "list", split_axis=0, concat_axis=0, tiled=True)

    first_cell = lax.axis_index("list") * cells_dev
    positions = jnp.arange(capacity, dtype=jnp.int32)
    scored = []
    for local in range(cells_dev):
        centroid = lax.dynamic_slice_in_dim(centroids, first_cell + local, 1, axis=0)
        residual = arrived[:, local] - centroid.reshape(1, 1, tile_rows, lanes)
        own_norm = jnp.sum(residual * residual, axis=(2, 3)).reshape(-1)
        residual = residual.reshape(list_size * slot_count, dim)
        rebuilt = rebuilt_slots(codebook_all, codes[local])
        slot_norm = jnp.sum(rebuilt * rebuilt, axis=1)
        cross = jnp.einsum(
            "sf,vf->sv", residual, rebuilt, precision=lax.Precision.HIGH
        )
        total = (own_norm[:, None] + slot_norm[None, :]) - 2.0 * cross
        valid = positions < cell_sizes[local]
        total = jnp.where(valid[None, :], total, jnp.zeros((), jnp.float32))
        scored.append(total.reshape(list_size, 1, slot_count * capacity // 128, 128))
    scored = jnp.stack(scored, axis=1)
    returned = lax.all_to_all(scored, "list", split_axis=0, concat_axis=0, tiled=True)
    returned = returned.reshape(cell_count * slot_count, capacity)
    picks = flat_cells * slot_count + slot_rank
    pick_hot = (
        picks[:, None] == jnp.arange(cell_count * slot_count, dtype=jnp.int32)[None, :]
    ).astype(jnp.bfloat16)
    picked = jnp.einsum(
        "pr,rf->pf", pick_hot, exact_parts(returned), preferred_element_type=jnp.float32
    )
    result = (
        picked[:, :capacity] + picked[:, capacity : 2 * capacity]
    ) + picked[:, 2 * capacity :]
    return result.reshape(query_rows, probe_count, capacity)


def solution(mesh):
    in_specs = (
        P(("query", "list"), None),
        P(("query", "list"), None),
        P(),
        P("query", None, None),
        P("list", None, None),
        P("list"),
    )
    out_specs = P(("query", "list"), None, None)
    return jax.shard_map(body, mesh=mesh, in_specs=in_specs, out_specs=out_specs, check_vma=False)
```
